128 devices in a mesh: blk: 64 (over z_lo, x, y, core), rep: 2 (over z_hi).
Axes of the slice: x: 4, y: 4, z: 4 (z_hi: 2, z_lo: 2; z = z_hi * 2 + z_lo), core: 2. Of those that a mesh axis runs over, the one named last changes fastest.
Arguments:
- features: bfloat16 [65536, 256], P('blk'), may hold values from -6 to 6
- weight: bfloat16 [256, 256], replicated, may hold values from -0.375 to 0.375
- bias: float32 [256], replicated, may hold values from -3 to 3
- cotangent: bfloat16 [65536, 256], P('blk'), may hold values from -6 to 6
- train_mask: int32 [65536], P('blk'), may hold values 0 or 1
- tile_cols: int32 [512, 16], P('blk', 'rep'), may hold values from -1 to 511, as said below
- tile_values: bfloat16 [512, 16, 128, 128], P('blk', 'rep'), as said below
Outputs:
- output: bfloat16 [65536, 256], P('blk')
- grad_in: bfloat16 [65536, 256], P('blk')
The draws below stay inside these ranges and needn't reach their ends.
Inputs may be any that keep to these rules, and one draw needn't show every extreme that they name: `tile_cols`: the live slots of a row tile name distinct column tiles, each in a slab at most 2 slabs from the row tile's slab around the loop of slabs (the last slab beside the first). In each half of a row tile's 16 slots (the first and the last 8) the live slots come first; some half of some row tile is full in every draw. `tile_values`: Nonnegative; the tile of an empty slot is all zeros.
All inputs are finite; a program needn't handle non-finite values. No bound on the sum of `train_mask` on one device may be relied on, other than what follows from the above.
Results may differ from the reference program's by a relative error of at most 0.0062.
Values may be sent and summed in bfloat16 or wider, within the bound.
No kernel may reach another device: no remote copies, remote signals or barrier semaphores. Data moves between devices by JAX's collectives and lax.ppermute only.
A program may use at most 64 MiB of HBM per device.

```python
import math
import jax
import jax.numpy as jnp
from jax import lax

F = 256
TILE = 128
NODE_DEV = 1024
SLOTS = 16
REACH = 2
NODES = 65536


def layout(key):
    base = jax.random.fold_in(key, 7)
    key_perm, key_count, key_full = jax.random.split(base, 3)
    tile_rows = NODES // TILE
    row_tiles = NODE_DEV // TILE
    loop_size = NODES // NODE_DEV
    window_tiles = (2 * REACH + 1) * row_tiles
    slot_half = SLOTS // 2

    def pick_row(row_key):
        return jax.random.permutation(row_key, window_tiles)
    row_keys = jax.random.split(key_perm, tile_rows)
    picked = jax.vmap(pick_row)(row_keys)[:, :SLOTS].astype(jnp.int32)
    slab = jnp.arange(tile_rows, dtype=jnp.int32)[:, None] // row_tiles
    column = jnp.mod(slab + picked // row_tiles - REACH, loop_size) * row_tiles + picked % row_tiles
    counts = jax.random.randint(key_count, (tile_rows * 2,), max(1, slot_half // 4), slot_half + 1)
    full_at = jax.random.randint(key_full, (), 0, tile_rows * 2)
    counts = counts.at[full_at].set(slot_half).reshape(tile_rows, 2)
    position = jnp.arange(SLOTS, dtype=jnp.int32) % slot_half
    halves = jnp.arange(SLOTS, dtype=jnp.int32) // slot_half
    live_mask = position[None, :] < counts[:, halves]
    return jnp.where(live_mask, column, -1).astype(jnp.int32)


def draw_tile_cols(key, part):
    return layout(key)


def draw_tile_values(key, part):
    live_mask = (layout(key) >= 0).astype(jnp.float32)
    key_mask, key_mag = jax.random.split(jax.random.fold_in(key, 11), 2)
    shape = (NODES // TILE, SLOTS, TILE, TILE)
    present = jax.random.bernoulli(key_mask, 0.5, shape).astype(jnp.float32)
    magnitude = jax.random.uniform(key_mag, shape, jnp.float32, 0.05, 1.0)
    factor = 1.0 / math.sqrt(SLOTS * TILE * 0.2)
    return (present * magnitude * factor * live_mask[:, :, None, None]).astype(jnp.bfloat16)


def plant(result, own_key, smallest, largest):
    extent = result.shape
    spot = [jax.random.randint(jax.random.fold_in(own_key, axis), (), 0, extent[axis]) for axis in range(len(extent))]
    result = result.at[tuple(spot)].set(smallest)
    longest = extent.index(max(extent))
    spot[longest] = (spot[longest] + 1) % extent[longest]
    return result.at[tuple(spot)].set(largest)


def block_levels(stream_key, extent, cuts, least, largest):
    def one(dim, parts):
        heights = jax.random.uniform(jax.random.fold_in(jax.random.fold_in(stream_key, 6), dim), (parts,), jnp.float32, least / len(cuts), largest / len(cuts))
        return jnp.repeat(jnp.exp(heights), extent[dim] // parts).reshape((-1,) + (1,) * (len(extent) - dim - 1))

    factor_of = one(*cuts[0])
    for cut in cuts[1:]:
        factor_of = factor_of * one(*cut)
    return factor_of


def bell_draw(own_key, dims, deviation, limit, shards=(), held_as=jnp.bfloat16):
    array = deviation * jax.random.normal(own_key, dims, jnp.float32)
    if shards:
        array = array * block_levels(own_key, dims, shards, -0.22, 0.18)
    return jnp.clip(array, -limit, limit).astype(held_as)


def setup_inputs(seed: int = 0) -> dict:
    key_of = jax.random.split(jax.random.key(seed), 8)
    features = bell_draw(key_of[0], (NODES, F), 1.0, 6.0, ((0, 64),))
    weight = bell_draw(key_of[1], (F, F), F ** -0.5, 0.375)
    bias = bell_draw(key_of[2], (F,), 0.5, 3.0, (), jnp.float32)
    cotangent = bell_draw(key_of[3], (NODES, F), 1.0, 6.0, ((0, 64),))
    train_mask = plant((jax.random.randint(key_of[4], (NODES,), 0, 2) < 1).astype(jnp.int32), jax.random.fold_in(key_of[4], 1), 0, 1)
    tile_cols = draw_tile_cols(jax.random.fold_in(key_of[7], 71), 0)
    tile_values = draw_tile_values(jax.random.fold_in(key_of[7], 71), 0)
    return dict(features=features, weight=weight, bias=bias, cotangent=cotangent, train_mask=train_mask, tile_cols=tile_cols, tile_values=tile_values)


def silu_grad(preact):
    sigmoid_z = jax.nn.sigmoid(preact)
    return sigmoid_z * (1.0 + preact * (1.0 - sigmoid_z))

def reference(features, weight, bias, cotangent, train_mask, tile_cols, tile_values):
    tile_rows = tile_cols.shape[0]
    tile_size = tile_values.shape[2]
    feat_width = weight.shape[1]
    projected = jnp.dot(features, weight, preferred_element_type=jnp.float32).astype(jnp.bfloat16)
    blocks = projected.reshape(tile_rows, tile_size, feat_width)
    live_mask = tile_cols >= 0
    safe_cols = jnp.where(live_mask, tile_cols, 0).astype(jnp.int32)

    def row_pre(row_args):
        row_cols, values = row_args
        gathered = blocks[row_cols].astype(jnp.float32)
        return jnp.einsum('sij,sjf->if', values.astype(jnp.float32), gathered)
    preact = lax.map(row_pre, (safe_cols, tile_values)).reshape(-1, feat_width) + bias
    output = jax.nn.silu(preact).astype(jnp.bfloat16)
    scaled = (train_mask.astype(jnp.float32)[:, None] * cotangent.astype(jnp.float32) * silu_grad(preact)).astype(jnp.bfloat16)
    scaled_blocks = scaled.reshape(tile_rows, tile_size, feat_width).astype(jnp.float32)

    def push(running, row_args):
        row_cols, row_live, values, row_grad = row_args
        products = jnp.einsum('sij,if->sjf', values.astype(jnp.float32), row_grad)
        products = products * row_live.astype(jnp.float32)[:, None, None]
        return (running.at[row_cols].add(products), None)
    running = jnp.zeros((tile_rows, tile_size, feat_width), jnp.float32)
    running, _ = lax.scan(push, running, (safe_cols, live_mask, tile_values, scaled_blocks))
    back_sum = running.reshape(-1, feat_width).astype(jnp.bfloat16)
    grad_in = jnp.dot(back_sum, weight.T, preferred_element_type=jnp.float32).astype(jnp.bfloat16)
    return (output, grad_in)
```

```python
import jax
import jax.numpy as jnp
from jax import lax
from jax.sharding import PartitionSpec as P

REACH = 2


def passed_along(array, axis, by):
    count = lax.axis_size(axis)
    return lax.ppermute(array, axis, [(i, (i + by) % count) for i in range(count)])


def swapped(array, axis):
    count = lax.axis_size(axis)
    return lax.ppermute(array, axis, [(i, i ^ 1) for i in range(count)])


def silu_grad(preact):
    sigmoid_z = jax.nn.sigmoid(preact)
    return sigmoid_z * (1.0 + preact * (1.0 - sigmoid_z))


def activate(preact, mask_rows, cot_rows):
    output = jax.nn.silu(preact).astype(jnp.bfloat16)
    scaled = (
        mask_rows.astype(jnp.float32)[:, None] * cot_rows.astype(jnp.float32) * silu_grad(preact)
    ).astype(jnp.bfloat16)
    return (output, scaled)


def shards(features, weight, bias, cotangent, train_mask, tile_cols, tile_values):
    row_count, feat_width = features.shape
    tile_size = tile_values.shape[2]
    row_tiles = row_count // tile_size
    loop_size = lax.axis_size("blk")
    position = lax.axis_index("blk")
    span = 2 * REACH + 1
    window_count = span * row_tiles

    live_mask = tile_cols >= 0
    offset = jnp.mod(tile_cols // row_tiles - position + REACH, loop_size)
    local_index = jnp.where(live_mask, offset * row_tiles + tile_cols % row_tiles, -1)
    picks = (local_index[:, :, None] == jnp.arange(window_count)[None, None, :]).astype(jnp.bfloat16)
    dense = jnp.einsum(
        "rsw,rsij->riwj", picks, tile_values, preferred_element_type=jnp.float32
    ).astype(jnp.bfloat16)
    dense = dense.reshape(row_count, span, row_count)

    projected = jnp.dot(features, weight, preferred_element_type=jnp.float32).astype(jnp.bfloat16)
    slabs = []
    for k in range(span):
        shift = k - REACH
        slabs.append(projected if shift == 0 else passed_along(projected, "blk", -shift))

    partial_value = jnp.dot(dense[:, REACH], slabs[REACH], preferred_element_type=jnp.float32)
    for k in range(span):
        if k != REACH:
            partial_value = partial_value + jnp.dot(
                dense[:, k], slabs[k], preferred_element_type=jnp.float32
            )
    preact = (partial_value + swapped(partial_value, "rep")) + bias
    output, scaled = activate(preact, train_mask, cotangent)

    gathered_sum = jnp.dot(dense[:, REACH].T, scaled, preferred_element_type=jnp.float32)
    for k in range(span):
        shift = k - REACH
        if shift != 0:
            piece = jnp.dot(dense[:, k].T, scaled, preferred_element_type=jnp.float32)
            gathered_sum = gathered_sum + passed_along(piece, "blk", shift)
    back_sum = (gathered_sum + swapped(gathered_sum, "rep")).astype(jnp.bfloat16)
    grad_in = jnp.dot(back_sum, weight.T, preferred_element_type=jnp.float32).astype(jnp.bfloat16)
    return (output, grad_in)


def solution(mesh):
    placed = (
        P("blk", None),
        P(),
        P(),
        P("blk", None),
        P("blk"),
        P("blk", "rep"),
        P("blk", "rep", None, None),
    )
    return jax.shard_map(
        shards,
        mesh=mesh,
        in_specs=placed,
        out_specs=(P("blk", None), P("blk", None)),
        check_vma=False,
    )
```

```python
import jax
import jax.numpy as jnp
from jax import lax
from jax.experimental import pallas as pl
from jax.experimental.pallas import tpu as pltpu
from jax.sharding import PartitionSpec as P

REACH = 2


def passed_along(array, axis, by):
    count = lax.axis_size(axis)
    return lax.ppermute(array, axis, [(i, (i + by) % count) for i in range(count)])


def swapped(array, axis):
    count = lax.axis_size(axis)
    return lax.ppermute(array, axis, [(i, i ^ 1) for i in range(count)])


def silu_grad(preact):
    sigmoid_z = jax.nn.sigmoid(preact)
    return sigmoid_z * (1.0 + preact * (1.0 - sigmoid_z))


def activate(preact, mask_rows, cot_rows):
    output = jax.nn.silu(preact).astype(jnp.bfloat16)
    scaled = (
        mask_rows.astype(jnp.float32)[:, None] * cot_rows.astype(jnp.float32) * silu_grad(preact)
    ).astype(jnp.bfloat16)
    return (output, scaled)


def dense_block(local_index, tile_values, window_count):
    row_tiles, slots, tile_size, _ = tile_values.shape

    def kernel(index_ref, values_ref, out_ref):
        r = pl.program_id(0)
        out_ref[...] = jnp.zeros_like(out_ref)
        for s in range(slots):
            w = index_ref[r, s]

            @pl.when((w >= 0) & (w < window_count))
            def _():
                start = pl.multiple_of(w * tile_size, tile_size)
                out_ref[:, pl.ds(start, tile_size)] = values_ref[0, s]

    return pl.pallas_call(
        kernel,
        grid_spec=pltpu.PrefetchScalarGridSpec(
            num_scalar_prefetch=1,
            grid=(row_tiles,),
            in_specs=[pl.BlockSpec((1, slots, tile_size, tile_size), lambda r, idx: (r, 0, 0, 0))],
            out_specs=pl.BlockSpec((tile_size, window_count * tile_size), lambda r, idx: (r, 0)),
        ),
        out_shape=jax.ShapeDtypeStruct((row_tiles * tile_size, window_count * tile_size), tile_values.dtype),
    )(local_index, tile_values)


def shards(features, weight, bias, cotangent, train_mask, tile_cols, tile_values):
    row_count, feat_width = features.shape
    tile_size = tile_values.shape[2]
    row_tiles = row_count // tile_size
    loop_size = lax.axis_size("blk")
    position = lax.axis_index("blk")
    span = 2 * REACH + 1
    window_count = span * row_tiles

    live_mask = tile_cols >= 0
    offset = jnp.mod(tile_cols // row_tiles - position + REACH, loop_size)
    local_index = jnp.where(live_mask, offset * row_tiles + tile_cols % row_tiles, -1)
    dense = dense_block(local_index, tile_values, window_count)
    blocks = [dense[:, k * row_count:(k + 1) * row_count] for k in range(span)]

    projected = jnp.dot(features, weight, preferred_element_type=jnp.float32).astype(jnp.bfloat16)
    slabs = []
    for k in range(span):
        shift = k - REACH
        slabs.append(projected if shift == 0 else passed_along(projected, "blk", -shift))

    partial_value = jnp.dot(blocks[REACH], slabs[REACH], preferred_element_type=jnp.float32)
    for k in range(span):
        if k != REACH:
            partial_value = partial_value + jnp.dot(blocks[k], slabs[k], preferred_element_type=jnp.float32)
    partial_value = partial_value.astype(jnp.bfloat16)
    preact = (
        partial_value.astype(jnp.float32) + swapped(partial_value, "rep").astype(jnp.float32)
    ) + bias
    output, scaled = activate(preact, train_mask, cotangent)

    contract_rows = (((0,), (0,)), ((), ()))
    gathered_sum = lax.dot_general(
        scaled, blocks[REACH], contract_rows, preferred_element_type=jnp.float32
    )
    for k in range(span):
        shift = k - REACH
        if shift != 0:
            piece = lax.dot_general(scaled, blocks[k], contract_rows, preferred_element_type=jnp.float32)
            gathered_sum = gathered_sum + passed_along(piece.astype(jnp.bfloat16), "blk", shift).astype(
                jnp.float32
            )
    gathered_sum = gathered_sum.astype(jnp.bfloat16)
    back_sum_t = (
        gathered_sum.astype(jnp.float32) + swapped(gathered_sum, "rep").astype(jnp.float32)
    ).astype(jnp.bfloat16)
    grad_in = lax.dot_general(
        back_sum_t, weight, (((0,), (1,)), ((), ())), preferred_element_type=jnp.float32
    ).astype(jnp.bfloat16)
    return (output, grad_in)


def solution(mesh):
    placed = (
        P("blk", None),
        P(),
        P(),
        P("blk", None),
        P("blk"),
        P("blk", "rep"),
        P("blk", "rep", None, None),
    )
    return jax.shard_map(
        shards,
        mesh=mesh,
        in_specs=placed,
        out_specs=(P("blk", None), P("blk", None)),
        check_vma=False,
    )
```

```python
import jax
import jax.numpy as jnp
from jax import lax
from jax.experimental import pallas as pl
from jax.experimental.pallas import tpu as pltpu
from jax.sharding import PartitionSpec as P

REACH = 2


def passed_along(array, axis, by):
    count = lax.axis_size(axis)
    return lax.ppermute(array, axis, [(i, (i + by) % count) for i in range(count)])


def swapped(array, axis):
    count = lax.axis_size(axis)
    return lax.ppermute(array, axis, [(i, i ^ 1) for i in range(count)])


def silu_grad(preact):
    sigmoid_z = jax.nn.sigmoid(preact)
    return sigmoid_z * (1.0 + preact * (1.0 - sigmoid_z))


def activate(preact, mask_rows, cot_rows):
    output = jax.nn.silu(preact).astype(jnp.bfloat16)
    scaled = (
        mask_rows.astype(jnp.float32)[:, None] * cot_rows.astype(jnp.float32) * silu_grad(preact)
    ).astype(jnp.bfloat16)
    return (output, scaled)


def dense_block(local_index, own_values, other_values, window_count):
    row_tiles, slots, tile_size, _ = own_values.shape

    def kernel(index_ref, own_ref, other_ref, out_ref):
        r = pl.program_id(0)
        out_ref[...] = jnp.zeros_like(out_ref)
        for half, values_ref in enumerate((own_ref, other_ref)):
            for s in range(slots):
                w = index_ref[r, half * slots + s]

                @pl.when((w >= 0) & (w < window_count))
                def _():
                    start = pl.multiple_of(w * tile_size, tile_size)
                    out_ref[:, pl.ds(start, tile_size)] = values_ref[0, s]

    tile_spec = pl.BlockSpec((1, slots, tile_size, tile_size), lambda r, idx: (r, 0, 0, 0))
    return pl.pallas_call(
        kernel,
        grid_spec=pltpu.PrefetchScalarGridSpec(
            num_scalar_prefetch=1,
            grid=(row_tiles,),
            in_specs=[tile_spec, tile_spec],
            out_specs=pl.BlockSpec((tile_size, window_count * tile_size), lambda r, idx: (r, 0)),
        ),
        out_shape=jax.ShapeDtypeStruct((row_tiles * tile_size, window_count * tile_size), own_values.dtype),
    )(local_index, own_values, other_values)


def shards(features, weight, bias, cotangent, train_mask, tile_cols, tile_values):
    row_count, feat_width = features.shape
    tile_size = tile_values.shape[2]
    row_tiles = row_count // tile_size
    half_tiles = row_tiles // 2
    half_rows = row_count // 2
    loop_size = lax.axis_size("blk")
    position = lax.axis_index("blk")
    side = lax.axis_index("rep")
    span = 2 * REACH + 1
    window_count = span * row_tiles

    tile_values = tile_values.reshape((2, half_tiles) + tile_values.shape[1:])
    tile_cols = tile_cols.reshape((2, half_tiles) + tile_cols.shape[1:])
    own_values = tile_values[side]
    other_values = swapped(tile_values[1 - side], "rep")
    own_cols = tile_cols[side]
    other_cols = swapped(tile_cols[1 - side], "rep")

    projected = jnp.dot(features, weight, preferred_element_type=jnp.float32).astype(jnp.bfloat16)
    slabs = []
    for k in range(span):
        shift = k - REACH
        slabs.append(projected if shift == 0 else passed_along(projected, "blk", -shift))

    cols = jnp.concatenate([own_cols, other_cols], axis=1)
    live_mask = cols >= 0
    offset = jnp.mod(cols // row_tiles - position + REACH, loop_size)
    local_index = jnp.where(live_mask, offset * row_tiles + cols % row_tiles, -1)
    dense = dense_block(local_index, own_values, other_values, window_count)
    blocks = [dense[:, k * row_count:(k + 1) * row_count] for k in range(span)]

    partial_value = jnp.dot(blocks[REACH], slabs[REACH], preferred_element_type=jnp.float32)
    for k in range(span):
        if k != REACH:
            partial_value = partial_value + jnp.dot(blocks[k], slabs[k], preferred_element_type=jnp.float32)
    preact = partial_value + bias
    mask_rows = lax.dynamic_slice_in_dim(train_mask, side * half_rows, half_rows)
    cot_rows = lax.dynamic_slice_in_dim(cotangent, side * half_rows, half_rows)
    own_output, scaled = activate(preact, mask_rows, cot_rows)
    other_output = swapped(own_output, "rep")
    output = jnp.concatenate(
        [jnp.where(side == 0, own_output, other_output), jnp.where(side == 0, other_output, own_output)], axis=0
    )

    contract_rows = (((0,), (0,)), ((), ()))
    gathered_sum = lax.dot_general(
        scaled, blocks[REACH], contract_rows, preferred_element_type=jnp.float32
    )
    for k in range(span):
        shift = k - REACH
        if shift != 0:
            piece = lax.dot_general(scaled, blocks[k], contract_rows, preferred_element_type=jnp.float32)
            gathered_sum = gathered_sum + passed_along(piece.astype(jnp.bfloat16), "blk", shift).astype(
                jnp.float32
            )
    gathered_sum = gathered_sum.astype(jnp.bfloat16)
    back_sum_t = (
        gathered_sum.astype(jnp.float32) + swapped(gathered_sum, "rep").astype(jnp.float32)
    ).astype(jnp.bfloat16)
    grad_in = lax.dot_general(
        back_sum_t, weight, (((0,), (1,)), ((), ())), preferred_element_type=jnp.float32
    ).astype(jnp.bfloat16)
    return (output, grad_in)


def solution(mesh):
    placed = (
        P("blk", None),
        P(),
        P(),
        P("blk", None),
        P("blk"),
        P("blk", "rep"),
        P("blk", "rep", None, None),
    )
    return jax.shard_map(
        shards,
        mesh=mesh,
        in_specs=placed,
        out_specs=(P("blk", None), P("blk", None)),
        check_vma=False,
    )
```

```python
import jax
import jax.numpy as jnp
from jax import lax
from jax.experimental import pallas as pl
from jax.experimental.pallas import tpu as pltpu
from jax.sharding import PartitionSpec as P

REACH = 2
FWD_T = jnp.float32
PIECE_T = jnp.float32
BACK_T = jnp.float32


def passed_along(array, axis, by):
    count = lax.axis_size(axis)
    return lax.ppermute(array, axis, [(i, (i + by) % count) for i in range(count)])


def swapped(array, axis):
    count = lax.axis_size(axis)
    return lax.ppermute(array, axis, [(i, i ^ 1) for i in range(count)])


def silu_grad(preact):
    sigmoid_z = jax.nn.sigmoid(preact)
    return sigmoid_z * (1.0 + preact * (1.0 - sigmoid_z))


def activate(preact, mask_rows, cot_rows):
    output = jax.nn.silu(preact).astype(jnp.bfloat16)
    scaled = (
        mask_rows.astype(jnp.float32)[:, None] * cot_rows.astype(jnp.float32) * silu_grad(preact)
    ).astype(jnp.bfloat16)
    return (output, scaled)


def dense_block(local_index, tile_values, window_count):
    row_tiles, slots, tile_size, _ = tile_values.shape

    def kernel(index_ref, values_ref, out_ref):
        r = pl.program_id(0)
        out_ref[...] = jnp.zeros_like(out_ref)
        for s in range(slots):
            w = index_ref[r, s]

            @pl.when((w >= 0) & (w < window_count))
            def _():
                start = pl.multiple_of(w * tile_size, tile_size)
                out_ref[:, pl.ds(start, tile_size)] = values_ref[0, s]

    return pl.pallas_call(
        kernel,
        grid_spec=pltpu.PrefetchScalarGridSpec(
            num_scalar_prefetch=1,
            grid=(row_tiles,),
            in_specs=[pl.BlockSpec((1, slots, tile_size, tile_size), lambda r, idx: (r, 0, 0, 0))],
            out_specs=pl.BlockSpec((tile_size, window_count * tile_size), lambda r, idx: (r, 0)),
        ),
        out_shape=jax.ShapeDtypeStruct((row_tiles * tile_size, window_count * tile_size), tile_values.dtype),
    )(local_index, tile_values)


def shards(features, weight, bias, cotangent, train_mask, tile_cols, tile_values):
    row_count, feat_width = features.shape
    tile_size = tile_values.shape[2]
    row_tiles = row_count // tile_size
    loop_size = lax.axis_size("blk")
    position = lax.axis_index("blk")
    span = 2 * REACH + 1
    window_count = span * row_tiles

    live_mask = tile_cols >= 0
    offset = jnp.mod(tile_cols // row_tiles - position + REACH, loop_size)
    local_index = jnp.where(live_mask, offset * row_tiles + tile_cols % row_tiles, -1)
    dense = dense_block(local_index, tile_values, window_count)
    blocks = [dense[:, k * row_count:(k + 1) * row_count] for k in range(span)]

    projected = jnp.dot(features, weight, preferred_element_type=jnp.float32).astype(jnp.bfloat16)
    slabs = []
    for k in range(span):
        shift = k - REACH
        slabs.append(projected if shift == 0 else passed_along(projected, "blk", -shift))

    partial_value = jnp.dot(blocks[REACH], slabs[REACH], preferred_element_type=jnp.float32)
    for k in range(span):
        if k != REACH:
            partial_value = partial_value + jnp.dot(blocks[k], slabs[k], preferred_element_type=jnp.float32)
    partial_value = partial_value.astype(FWD_T)
    preact = (
        partial_value.astype(jnp.float32) + swapped(partial_value, "rep").astype(jnp.float32)
    ) + bias
    output, scaled = activate(preact, train_mask, cotangent)

    contract_rows = (((0,), (0,)), ((), ()))
    gathered_sum = lax.dot_general(
        scaled, blocks[REACH], contract_rows, preferred_element_type=jnp.float32
    )
    for k in range(span):
        shift = k - REACH
        if shift != 0:
            piece = lax.dot_general(scaled, blocks[k], contract_rows, preferred_element_type=jnp.float32)
            gathered_sum = gathered_sum + passed_along(piece.astype(PIECE_T), "blk", shift).astype(
                jnp.float32
            )
    gathered_sum = gathered_sum.astype(BACK_T)
    back_sum_t = (
        gathered_sum.astype(jnp.float32) + swapped(gathered_sum, "rep").astype(jnp.float32)
    ).astype(jnp.bfloat16)
    grad_in = lax.dot_general(
        back_sum_t, weight, (((0,), (1,)), ((), ())), preferred_element_type=jnp.float32
    ).astype(jnp.bfloat16)
    return (output, grad_in)


def solution(mesh):
    placed = (
        P("blk", None),
        P(),
        P(),
        P("blk", None),
        P("blk"),
        P("blk", "rep"),
        P("blk", "rep", None, None),
    )
    return jax.shard_map(
        shards,
        mesh=mesh,
        in_specs=placed,
        out_specs=(P("blk", None), P("blk", None)),
        check_vma=False,
    )
```

```python
import jax
import jax.numpy as jnp
from jax import lax
from jax.experimental import pallas as pl
from jax.experimental.pallas import tpu as pltpu
from jax.sharding import PartitionSpec as P

REACH = 2


def passed_along(array, axis, by):
    count = lax.axis_size(axis)
    return lax.ppermute(array, axis, [(i, (i + by) % count) for i in range(count)])


def paired(array, axis, even_by, odd_by):
    count = lax.axis_size(axis)
    return lax.ppermute(
        array, axis, [(i, (i + (even_by if i % 2 == 0 else odd_by)) % count) for i in range(count)]
    )


def swapped(array, axis):
    count = lax.axis_size(axis)
    return lax.ppermute(array, axis, [(i, i ^ 1) for i in range(count)])


def silu_grad(preact):
    sigmoid_z = jax.nn.sigmoid(preact)
    return sigmoid_z * (1.0 + preact * (1.0 - sigmoid_z))


def activate(preact, mask_rows, cot_rows):
    output = jax.nn.silu(preact).astype(jnp.bfloat16)
    scaled = (
        mask_rows.astype(jnp.float32)[:, None] * cot_rows.astype(jnp.float32) * silu_grad(preact)
    ).astype(jnp.bfloat16)
    return (output, scaled)


def dense_block(local_index, tile_values, window_count):
    row_tiles, slots, tile_size, _ = tile_values.shape

    def kernel(index_ref, values_ref, out_ref):
        r = pl.program_id(0)
        out_ref[...] = jnp.zeros_like(out_ref)
        for s in range(slots):
            w = index_ref[r, s]

            @pl.when((w >= 0) & (w < window_count))
            def _():
                start = pl.multiple_of(w * tile_size, tile_size)
                out_ref[:, pl.ds(start, tile_size)] = values_ref[0, s]

    return pl.pallas_call(
        kernel,
        grid_spec=pltpu.PrefetchScalarGridSpec(
            num_scalar_prefetch=1,
            grid=(row_tiles,),
            in_specs=[pl.BlockSpec((1, slots, tile_size, tile_size), lambda r, idx: (r, 0, 0, 0))],
            out_specs=pl.BlockSpec((tile_size, window_count * tile_size), lambda r, idx: (r, 0)),
        ),
        out_shape=jax.ShapeDtypeStruct((row_tiles * tile_size, window_count * tile_size), tile_values.dtype),
    )(local_index, tile_values)


def shards(features, weight, bias, cotangent, train_mask, tile_cols, tile_values):
    row_count, feat_width = features.shape
    tile_size = tile_values.shape[2]
    row_tiles = row_count // tile_size
    loop_size = lax.axis_size("blk")
    position = lax.axis_index("blk")
    span = 2 * REACH + 1
    window_count = span * row_tiles

    toward = 1 - 2 * (position % 2)
    live_mask = tile_cols >= 0
    offset = jnp.mod(tile_cols // row_tiles - position + REACH, loop_size) - REACH
    relative = offset * toward
    order = jnp.where(relative >= 0, relative, REACH - relative)
    local_index = jnp.where(live_mask, order * row_tiles + tile_cols % row_tiles, -1)
    dense = dense_block(local_index, tile_values, window_count)
    blocks = [dense[:, k * row_count:(k + 1) * row_count] for k in range(span)]

    projected = jnp.dot(features, weight, preferred_element_type=jnp.float32).astype(jnp.bfloat16)
    slabs = [
        projected,
        paired(projected, "blk", 1, -1),
        paired(projected, "blk", -2, 2),
        paired(projected, "blk", -1, 1),
        paired(projected, "blk", 2, -2),
    ]

    partial_value = jnp.dot(blocks[0], slabs[0], preferred_element_type=jnp.float32)
    for k in range(1, span):
        partial_value = partial_value + jnp.dot(blocks[k], slabs[k], preferred_element_type=jnp.float32)
    preact = (partial_value + swapped(partial_value, "rep")) + bias
    output, scaled = activate(preact, train_mask, cotangent)

    contract_rows = (((0,), (0,)), ((), ()))
    pieces = [
        lax.dot_general(scaled, blocks[k], contract_rows, preferred_element_type=jnp.float32)
        for k in range(span)
    ]
    from_partner = paired(jnp.stack([pieces[1], pieces[2]]), "blk", 1, -1)
    far = paired(pieces[4], "blk", -2, 2)
    near = paired(pieces[3] + from_partner[1], "blk", -1, 1)
    gathered_sum = pieces[0] + from_partner[0] + near + far
    back_sum_t = (gathered_sum + swapped(gathered_sum, "rep")).astype(jnp.bfloat16)
    grad_in = lax.dot_general(
        back_sum_t, weight, (((0,), (1,)), ((), ())), preferred_element_type=jnp.float32
    ).astype(jnp.bfloat16)
    return (output, grad_in)


def solution(mesh):
    placed = (
        P("blk", None),
        P(),
        P(),
        P("blk", None),
        P("blk"),
        P("blk", "rep"),
        P("blk", "rep", None, None),
    )
    return jax.shard_map(
        shards,
        mesh=mesh,
        in_specs=placed,
        out_specs=(P("blk", None), P("blk", None)),
        check_vma=False,
    )
```

```python
import jax
import jax.numpy as jnp
from jax import lax
from jax.experimental import pallas as pl
from jax.experimental.pallas import tpu as pltpu
from jax.sharding import PartitionSpec as P

REACH = 2


def passed_along(array, axis, by):
    count = lax.axis_size(axis)
    return lax.ppermute(array, axis, [(i, (i + by) % count) for i in range(count)])


def paired(array, axis, even_by, odd_by):
    count = lax.axis_size(axis)
    return lax.ppermute(
        array, axis, [(i, (i + (even_by if i % 2 == 0 else odd_by)) % count) for i in range(count)]
    )


def swapped(array, axis):
    count = lax.axis_size(axis)
    return lax.ppermute(array, axis, [(i, i ^ 1) for i in range(count)])


def silu_grad(preact):
    sigmoid_z = jax.nn.sigmoid(preact)
    return sigmoid_z * (1.0 + preact * (1.0 - sigmoid_z))


def activate(preact, mask_rows, cot_rows):
    output = jax.nn.silu(preact).astype(jnp.bfloat16)
    scaled = (
        mask_rows.astype(jnp.float32)[:, None] * cot_rows.astype(jnp.float32) * silu_grad(preact)
    ).astype(jnp.bfloat16)
    return (output, scaled)


def dense_block(local_index, tile_values, window_count):
    row_tiles, slots, tile_size, _ = tile_values.shape

    def kernel(index_ref, values_ref, out_ref):
        r = pl.program_id(0)
        out_ref[...] = jnp.zeros_like(out_ref)
        for s in range(slots):
            w = index_ref[r, s]

            @pl.when((w >= 0) & (w < window_count))
            def _():
                start = pl.multiple_of(w * tile_size, tile_size)
                out_ref[:, pl.ds(start, tile_size)] = values_ref[0, s]

    return pl.pallas_call(
        kernel,
        grid_spec=pltpu.PrefetchScalarGridSpec(
            num_scalar_prefetch=1,
            grid=(row_tiles,),
            in_specs=[pl.BlockSpec((1, slots, tile_size, tile_size), lambda r, idx: (r, 0, 0, 0))],
            out_specs=pl.BlockSpec((tile_size, window_count * tile_size), lambda r, idx: (r, 0)),
        ),
        out_shape=jax.ShapeDtypeStruct((row_tiles * tile_size, window_count * tile_size), tile_values.dtype),
    )(local_index, tile_values)


def shards(features, weight, bias, cotangent, train_mask, tile_cols, tile_values):
    row_count, feat_width = features.shape
    tile_size = tile_values.shape[2]
    row_tiles = row_count // tile_size
    loop_size = lax.axis_size("blk")
    position = lax.axis_index("blk")
    span = 2 * REACH + 1
    window_count = span * row_tiles

    toward = 1 - 2 * (position % 2)
    live_mask = tile_cols >= 0
    offset = jnp.mod(tile_cols // row_tiles - position + REACH, loop_size) - REACH
    relative = offset * toward
    order = jnp.where(relative >= 0, relative, REACH - relative)
    local_index = jnp.where(live_mask, order * row_tiles + tile_cols % row_tiles, -1)
    dense = dense_block(local_index, tile_values, window_count)
    blocks = [dense[:, k * row_count:(k + 1) * row_count] for k in range(span)]

    projected = jnp.dot(features, weight, preferred_element_type=jnp.float32).astype(jnp.bfloat16)
    slabs = [
        projected,
        paired(projected, "blk", 1, -1),
        paired(projected, "blk", -2, 2),
        paired(projected, "blk", -1, 1),
        paired(projected, "blk", 2, -2),
    ]

    partial_value = jnp.dot(blocks[0], slabs[0], preferred_element_type=jnp.float32)
    for k in range(1, span):
        partial_value = partial_value + jnp.dot(blocks[k], slabs[k], preferred_element_type=jnp.float32)
    preact = (partial_value + swapped(partial_value, "rep")) + bias
    output, scaled = activate(preact, train_mask, cotangent)

    contract_rows = (((0,), (0,)), ((), ()))
    pieces = [
        lax.dot_general(scaled, blocks[k], contract_rows, preferred_element_type=jnp.float32)
        for k in (0, 3, 4)
    ]
    partner_pieces = lax.dot_general(
        scaled, dense[:, row_count:3 * row_count], contract_rows, preferred_element_type=jnp.float32
    )
    from_partner = paired(partner_pieces, "blk", 1, -1)
    far = paired(pieces[2], "blk", -2, 2)
    near = paired(pieces[1] + from_partner[:, row_count:], "blk", -1, 1)
    gathered_sum = pieces[0] + from_partner[:, :row_count] + near + far
    half_rows = row_count // 2
    side = lax.axis_index("rep")
    kept = lax.dynamic_slice_in_dim(gathered_sum, side * half_rows, half_rows, axis=1)
    sent = lax.dynamic_slice_in_dim(gathered_sum, (1 - side) * half_rows, half_rows, axis=1)
    back_half = (kept + swapped(sent, "rep")).astype(jnp.bfloat16)
    own_grad = lax.dot_general(
        back_half, weight, (((0,), (1,)), ((), ())), preferred_element_type=jnp.float32
    ).astype(jnp.bfloat16)
    other_grad = swapped(own_grad, "rep")
    grad_in = jnp.concatenate(
        [jnp.where(side == 0, own_grad, other_grad), jnp.where(side == 0, other_grad, own_grad)], axis=0
    )
    return (output, grad_in)


def solution(mesh):
    placed = (
        P("blk", None),
        P(),
        P(),
        P("blk", None),
        P("blk"),
        P("blk", "rep"),
        P("blk", "rep", None, None),
    )
    return jax.shard_map(
        shards,
        mesh=mesh,
        in_specs=placed,
        out_specs=(P("blk", None), P("blk", None)),
        check_vma=False,
    )
```
